1024 devices in a mesh: fsdp: 8 (over x, y_hi), ctx: 32 (over z, core), head: 4 (over y_lo).
Axes of the slice: x: 4, y: 8 (y_hi: 2, y_lo: 4; y = y_hi * 4 + y_lo), z: 16, core: 2. Of those that a mesh axis runs over, the one named last changes fastest.
Arguments:
- q_raw: bfloat16 [8, 4096, 4096], P('fsdp', 'ctx', 'head'), may hold values from -6 to 6
- unnormed_keys: bfloat16 [8, 4096, 2048], P('fsdp', 'ctx', 'head'), may hold values from -6 to 6
- value_input: bfloat16 [8, 4096, 2048], P('fsdp', 'ctx', 'head'), may hold values from -6 to 6
- d_out: bfloat16 [8, 4096, 4096], P('fsdp', 'ctx', 'head'), may hold values from -6 to 6
- file_ids: int32 [8, 4096], P('fsdp', 'ctx'), may hold values from 0 to 15, never falling along the last dimension, each value on 1 to 512 neighbouring positions
- q_gain: float32 [128], replicated, may hold values from 0.5 to 2.5
- k_gain: float32 [128], replicated, may hold values from 0.4 to 2.2
Outputs:
- attended: bfloat16 [8, 4096, 4096], P('fsdp', 'ctx', 'head')
- dq_raw: bfloat16 [8, 4096, 4096], P('fsdp', 'ctx', 'head')
- dk_raw: bfloat16 [8, 4096, 2048], P('fsdp', 'ctx', 'head')
- dv: bfloat16 [8, 4096, 2048], P('fsdp', 'ctx', 'head')
- dq_gain: float32 [128], replicated
- dk_gain: float32 [128], replicated
The draws below stay inside these ranges and needn't reach their ends.
Inputs may be any that keep to these rules, and one draw needn't show every extreme that they name: `file_ids`: in each sequence the file numbers never fall, every file number from 0 up occurs, every file has 1 to min(4095, 512) tokens, and some file has exactly that many.
All inputs are finite; a program needn't handle non-finite values.
Results may differ from the reference program's by a relative error of at most 0.013.
Values may be sent and summed in bfloat16 or wider, within the bound.
No kernel may reach another device: no remote copies, remote signals or barrier semaphores. Data moves between devices by JAX's collectives and lax.ppermute only.
A program may use at most 32 MiB of HBM per device.

```python
import math
import jax
import jax.numpy as jnp
import numpy as np
from jax import lax

HQ = 32
KEY_VALUE_HEADS = 16
HEAD_WIDTH = 128
WINDOW = 256
QPAS = 168
SEQUENCE_LENGTH = 4096
SEQUENCE_COUNT = 8


def steps_of(key, dims, cuts, least, high):
    factor_of, own = 1.0, jax.random.fold_in(key, 6)
    for position, shards_of in cuts:
        steps = jnp.exp(jax.random.uniform(jax.random.fold_in(own, position), (shards_of,), jnp.float32, least / len(cuts), high / len(cuts)))
        factor_of = factor_of * jnp.repeat(steps, dims[position] // shards_of).reshape([-1 if axis == position else 1 for axis in range(len(dims))])
    return factor_of


def length_profile(number_of, total, reach, skew):
    loads = [(1 << 20) // math.isqrt(grade ** skew) + 1 for grade in range(2, number_of + 1)]
    surplus, given = total - reach - (number_of - 1), [1] * (number_of - 1)
    while surplus > 0:
        candidates = [i for i in range(number_of - 1) if given[i] < reach]
        whole, left = sum([loads[i] for i in candidates]), surplus
        for i in candidates:
            addition = min(reach - given[i], max(1, left * loads[i] // whole), surplus)
            given[i] = given[i] + addition
            surplus = surplus - addition
    return np.array([reach] + given)


def ragged(own_key, count, total, bound, lean):
    if count == 2:
        one = jax.random.randint(own_key, (), max(1, total - bound), min(bound, total - 1) + 1)
        return jnp.stack([one, total - one])
    tallies = jnp.asarray(length_profile(count, total, bound, lean), jnp.int32)
    twos = (count - 1) // 2
    source_of, taker = tallies[1:1 + 2 * twos:2], tallies[2:2 + 2 * twos:2]
    margin = jnp.minimum(source_of - 1, bound - taker)
    moved = jax.random.randint(jax.random.fold_in(own_key, 1), (twos,), 0, 1 << 20) % (margin + 1)
    tallies = tallies.at[1:1 + 2 * twos:2].set(source_of - moved).at[2:2 + 2 * twos:2].set(taker + moved)
    return tallies[jax.random.permutation(jax.random.fold_in(own_key, 2), count)]


def bell_draw(key, shape, deviation, reach, split=(), kind=jnp.bfloat16):
    drawn = deviation * jax.random.normal(key, shape, jnp.float32)
    if split:
        drawn = drawn * steps_of(key, shape, split, -0.22, 0.18)
    return jnp.clip(drawn, -reach, reach).astype(kind)


def setup_inputs(seed: int = 0) -> dict:
    keys = jax.random.split(jax.random.key(seed), 8)
    return {
        "q_raw": bell_draw(keys[0], (SEQUENCE_COUNT, SEQUENCE_LENGTH, HQ * HEAD_WIDTH), 1.0, 6.0, ((0, 8), (1, 32), (2, 4))),
        "unnormed_keys": bell_draw(keys[1], (SEQUENCE_COUNT, SEQUENCE_LENGTH, KEY_VALUE_HEADS * HEAD_WIDTH), 1.0, 6.0, ((0, 8), (1, 32), (2, 4))),
        "value_input": bell_draw(keys[2], (SEQUENCE_COUNT, SEQUENCE_LENGTH, KEY_VALUE_HEADS * HEAD_WIDTH), 1.0, 6.0, ((0, 8), (1, 32), (2, 4))),
        "d_out": bell_draw(keys[3], (SEQUENCE_COUNT, SEQUENCE_LENGTH, HQ * HEAD_WIDTH), 1.0, 6.0, ((0, 8), (1, 32), (2, 4))),
        "file_ids": jax.vmap(lambda own: jnp.searchsorted(jnp.cumsum(ragged(own, max(2, SEQUENCE_LENGTH // WINDOW), SEQUENCE_LENGTH, min(SEQUENCE_LENGTH - 1, 2 * WINDOW), 1)), jnp.arange(SEQUENCE_LENGTH), side="right"))(jax.random.split(keys[4], SEQUENCE_COUNT)).reshape((SEQUENCE_COUNT, SEQUENCE_LENGTH)).astype(jnp.int32),
        "q_gain": jnp.clip(jax.random.uniform(keys[5], (HEAD_WIDTH,), jnp.float32, 0.5, 2.5), 0.5, 2.5),
        "k_gain": jnp.clip(jax.random.uniform(keys[6], (HEAD_WIDTH,), jnp.float32, 0.4, 2.2), 0.4, 2.2),
    }


EPSILON = 1e-06
THETA_BASE = 10000.0
NEGATIVE = -1e+30

def rotate(values, positions):
    half_dim = values.shape[-1] // 2
    frequency = THETA_BASE ** (-(jnp.arange(half_dim, dtype=jnp.float32) * 2.0 / values.shape[-1]))
    angles = positions.astype(jnp.float32)[:, None] * frequency[None, :]
    cosine = jnp.cos(angles)[:, None, :]
    sine_part = jnp.sin(angles)[:, None, :]
    first_half = values[..., :half_dim]
    second = values[..., half_dim:]
    return jnp.concatenate([first_half * cosine - second * sine_part, second * cosine + first_half * sine_part], axis=-1)

def unrotate(values, positions):
    half_dim = values.shape[-1] // 2
    frequency = THETA_BASE ** (-(jnp.arange(half_dim, dtype=jnp.float32) * 2.0 / values.shape[-1]))
    angles = positions.astype(jnp.float32)[:, None] * frequency[None, :]
    cosine = jnp.cos(angles)[:, None, :]
    sine_part = jnp.sin(angles)[:, None, :]
    first_half = values[..., :half_dim]
    second = values[..., half_dim:]
    return jnp.concatenate([first_half * cosine + second * sine_part, second * cosine - first_half * sine_part], axis=-1)

def normalize(raw_rows, gain_row, positions, head_count):
    values = raw_rows.astype(jnp.float32).reshape(raw_rows.shape[0], head_count, -1)
    inverse = lax.rsqrt(lax.optimization_barrier(jnp.mean(values * values, axis=-1, keepdims=True)) + EPSILON)
    unit_rows = values * inverse
    return (unit_rows, inverse, rotate(unit_rows * gain_row, positions).astype(jnp.bfloat16))

def restore(grad_rot, unit_rows, inverse, gain_row, positions):
    normed = unrotate(grad_rot, positions)
    gain_term = lax.optimization_barrier(jnp.sum(normed * unit_rows, axis=(0, 1)))
    scaled = normed * gain_row
    grad_raw = inverse * (scaled - unit_rows * lax.optimization_barrier(jnp.mean(scaled * unit_rows, axis=-1, keepdims=True)))
    return (grad_raw, gain_term)

def visible(query_pos, query_file, key_pos, key_file):
    earlier = key_pos[None, :] <= query_pos[:, None]
    inside = query_pos[:, None] - key_pos[None, :] < WINDOW
    same_file = key_file[None, :] == query_file[:, None]
    return earlier & inside & same_file & (key_pos[None, :] >= 0)

def block_math(queries, out_grads, key_rows, value_rows, allowed):
    scale_factor = QPAS ** (-0.5)
    logit_scores = scale_factor * jnp.einsum('qhgd,khd->hgqk', queries.astype(jnp.float32), key_rows.astype(jnp.float32))
    logit_scores = jnp.where(allowed[None, None], logit_scores, NEGATIVE)
    row_peak = lax.optimization_barrier(jnp.max(logit_scores, axis=-1, keepdims=True))
    log_total = row_peak + jnp.log(lax.optimization_barrier(jnp.sum(jnp.exp(logit_scores - row_peak), axis=-1, keepdims=True)))
    weights = jnp.exp(logit_scores - log_total)
    weights_low = weights.astype(jnp.bfloat16)
    attended = jnp.einsum('hgqk,khd->qhgd', weights_low.astype(jnp.float32), value_rows.astype(jnp.float32)).astype(jnp.bfloat16)
    row_delta = jnp.transpose(lax.optimization_barrier(jnp.sum(out_grads.astype(jnp.float32) * attended.astype(jnp.float32), axis=-1)), (1, 2, 0))
    dprobs = jnp.einsum('qhgd,khd->hgqk', out_grads.astype(jnp.float32), value_rows.astype(jnp.float32))
    dscores = (weights * (dprobs - row_delta[..., None])).astype(jnp.bfloat16)
    grad_queries = scale_factor * jnp.einsum('hgqk,khd->qhgd', dscores.astype(jnp.float32), key_rows.astype(jnp.float32))
    grad_keys = scale_factor * jnp.einsum('hgqk,qhgd->khd', dscores.astype(jnp.float32), queries.astype(jnp.float32))
    grad_values = jnp.einsum('hgqk,qhgd->khd', weights_low.astype(jnp.float32), out_grads.astype(jnp.float32))
    return (attended, grad_queries, grad_keys, grad_values)

def sequence(q_raw, unnormed_keys, value_input, d_out, file_row, q_gain, k_gain):
    length = q_raw.shape[0]
    heads_q = q_raw.shape[1] // HEAD_WIDTH
    heads_kv = unnormed_keys.shape[1] // HEAD_WIDTH
    group_size = heads_q // heads_kv
    positions = jnp.arange(length, dtype=jnp.int32)
    q_unit, q_inv, q_rot = normalize(q_raw, q_gain, positions, heads_q)
    k_unit, k_inv, k_rot = normalize(unnormed_keys, k_gain, positions, heads_kv)
    pad_keys = jnp.concatenate([jnp.zeros((WINDOW, heads_kv, HEAD_WIDTH), jnp.bfloat16), k_rot], axis=0)
    pad_values = jnp.concatenate([jnp.zeros((WINDOW, heads_kv, HEAD_WIDTH), jnp.bfloat16), value_input.reshape(length, heads_kv, HEAD_WIDTH)], axis=0)
    pad_files = jnp.concatenate([jnp.full((WINDOW,), -1, jnp.int32), file_row.astype(jnp.int32)], axis=0)
    pad_pos = jnp.arange(WINDOW + length, dtype=jnp.int32) - WINDOW
    queries = q_rot.reshape(length, heads_kv, group_size, HEAD_WIDTH)
    out_grads = d_out.reshape(length, heads_kv, group_size, HEAD_WIDTH)
    block_rows = min(512, length)
    block_count = length // block_rows
    key_span = WINDOW + block_rows

    def one_block(totals, block_index):
        key_acc, value_acc = totals
        first_row = (block_index * block_rows).astype(jnp.int32)
        q_block = lax.dynamic_slice_in_dim(queries, first_row, block_rows, 0)
        g_block = lax.dynamic_slice_in_dim(out_grads, first_row, block_rows, 0)
        q_pos = lax.dynamic_slice_in_dim(positions, first_row, block_rows, 0)
        q_file = lax.dynamic_slice_in_dim(file_row.astype(jnp.int32), first_row, block_rows, 0)
        key_block = lax.dynamic_slice_in_dim(pad_keys, first_row, key_span, 0)
        value_block = lax.dynamic_slice_in_dim(pad_values, first_row, key_span, 0)
        key_pos = lax.dynamic_slice_in_dim(pad_pos, first_row, key_span, 0)
        key_file = lax.dynamic_slice_in_dim(pad_files, first_row, key_span, 0)
        allowed = visible(q_pos, q_file, key_pos, key_file)
        attended, grad_queries, grad_keys, grad_values = block_math(q_block, g_block, key_block, value_block, allowed)
        key_acc = lax.dynamic_update_slice_in_dim(key_acc, lax.dynamic_slice_in_dim(key_acc, first_row, key_span, 0) + grad_keys, first_row, 0)
        value_acc = lax.dynamic_update_slice_in_dim(value_acc, lax.dynamic_slice_in_dim(value_acc, first_row, key_span, 0) + grad_values, first_row, 0)
        return ((key_acc, value_acc), (attended, grad_queries))
    empty = jnp.zeros((WINDOW + length, heads_kv, HEAD_WIDTH), jnp.float32)
    (key_acc, value_acc), (attended, grad_queries) = lax.scan(one_block, (empty, empty), jnp.arange(block_count, dtype=jnp.int32))
    attended = attended.reshape(length, heads_q * HEAD_WIDTH)
    grad_queries = grad_queries.reshape(length, heads_q, HEAD_WIDTH)
    dq_raw, q_term = restore(grad_queries, q_unit, q_inv, q_gain, positions)
    dk_raw, k_term = restore(key_acc[WINDOW:], k_unit, k_inv, k_gain, positions)
    return (attended, dq_raw.astype(jnp.bfloat16).reshape(length, -1), dk_raw.astype(jnp.bfloat16).reshape(length, -1), value_acc[WINDOW:].astype(jnp.bfloat16).reshape(length, -1), q_term, k_term)

def reference(q_raw, unnormed_keys, value_input, d_out, file_ids, q_gain, k_gain):
    results = lax.map(lambda sequence_items: sequence(*sequence_items, q_gain, k_gain), (q_raw, unnormed_keys, value_input, d_out, file_ids))
    return (results[0], results[1], results[2], results[3], lax.optimization_barrier(jnp.sum(results[4], axis=0)), lax.optimization_barrier(jnp.sum(results[5], axis=0)))
```

```python
import jax
import jax.numpy as jnp
from jax import lax
from jax.sharding import PartitionSpec as P

HEAD_WIDTH = 128
WINDOW = 256
QPAS = 168


EPSILON = 1e-06
THETA_BASE = 10000.0
NEGATIVE = -1e30


def passed_along(value, axis, by):
    devices = lax.axis_size(axis)
    pairs = [(i, i + by) for i in range(devices) if 0 <= i + by < devices]
    return lax.ppermute(value, axis, pairs)


def butterfly_sum(value, axis):
    devices = lax.axis_size(axis)
    stride = 1
    while stride < devices:
        pairs = [(i, i ^ stride) for i in range(devices)]
        value = value + lax.ppermute(value, axis, pairs)
        stride *= 2
    return value


def rotate(values, positions):
    half_dim = values.shape[-1] // 2
    frequency = THETA_BASE ** (-(jnp.arange(half_dim, dtype=jnp.float32) * 2.0 / values.shape[-1]))
    angles = positions.astype(jnp.float32)[:, None] * frequency[None, :]
    cosine = jnp.cos(angles)[:, None, :]
    sine_part = jnp.sin(angles)[:, None, :]
    first_half = values[..., :half_dim]
    second = values[..., half_dim:]
    return jnp.concatenate(
        [first_half * cosine - second * sine_part, second * cosine + first_half * sine_part],
        axis=-1,
    )


def unrotate(values, positions):
    half_dim = values.shape[-1] // 2
    frequency = THETA_BASE ** (-(jnp.arange(half_dim, dtype=jnp.float32) * 2.0 / values.shape[-1]))
    angles = positions.astype(jnp.float32)[:, None] * frequency[None, :]
    cosine = jnp.cos(angles)[:, None, :]
    sine_part = jnp.sin(angles)[:, None, :]
    first_half = values[..., :half_dim]
    second = values[..., half_dim:]
    return jnp.concatenate(
        [first_half * cosine + second * sine_part, second * cosine - first_half * sine_part],
        axis=-1,
    )


def normalize(raw_rows, gain_row, positions, head_count):
    values = raw_rows.astype(jnp.float32).reshape(raw_rows.shape[0], head_count, -1)
    inverse = lax.rsqrt(jnp.mean(values * values, axis=-1, keepdims=True) + EPSILON)
    unit_rows = values * inverse
    return (unit_rows, inverse, rotate(unit_rows * gain_row, positions).astype(jnp.bfloat16))


def restore(grad_rot, unit_rows, inverse, gain_row, positions):
    normed = unrotate(grad_rot, positions)
    gain_term = jnp.sum(normed * unit_rows, axis=(0, 1))
    scaled = normed * gain_row
    grad_raw = inverse * (scaled - unit_rows * jnp.mean(scaled * unit_rows, axis=-1, keepdims=True))
    return (grad_raw, gain_term)


def visible(query_pos, query_file, key_pos, key_file):
    earlier = key_pos[None, :] <= query_pos[:, None]
    inside = query_pos[:, None] - key_pos[None, :] < WINDOW
    same_file = key_file[None, :] == query_file[:, None]
    return earlier & inside & same_file & (key_pos[None, :] >= 0)


def scores_of(queries, key_rows, allowed):
    logit_scores = QPAS ** (-0.5) * jnp.einsum(
        "qhgd,khd->hgqk", queries, key_rows, preferred_element_type=jnp.float32
    )
    return jnp.where(allowed[None, None], logit_scores, NEGATIVE)


def body(q_raw, unnormed_keys, value_input, d_out, file_ids, q_gain, k_gain):
    row_count = q_raw.shape[1]
    qheads = q_raw.shape[2] // HEAD_WIDTH
    kheads = unnormed_keys.shape[2] // HEAD_WIDTH
    group_size = qheads // kheads
    ctx_size = lax.axis_size("ctx")
    ctx_place = lax.axis_index("ctx")
    reach_count = min((WINDOW + row_count - 1) // row_count, ctx_size - 1)
    scale_factor = QPAS ** (-0.5)
    positions = ctx_place * row_count + jnp.arange(row_count, dtype=jnp.int32)
    file_row = file_ids[0]
    q_unit, q_inv, q_rot = normalize(q_raw[0], q_gain, positions, qheads)
    k_unit, k_inv, k_rot = normalize(unnormed_keys[0], k_gain, positions, kheads)
    value_own = value_input[0].reshape(row_count, kheads, HEAD_WIDTH)
    key_list, value_list, file_list = ([], [], [])
    for offset in range(reach_count, 0, -1):
        key_far, value_far, file_far = passed_along((k_rot, value_own, file_row), "ctx", offset)
        key_list.append(key_far)
        value_list.append(value_far)
        file_list.append(file_far)
    key_rows = jnp.concatenate(key_list + [k_rot], axis=0)
    value_rows = jnp.concatenate(value_list + [value_own], axis=0)
    key_files = jnp.concatenate(file_list + [file_row], axis=0)
    key_pos = (ctx_place - reach_count) * row_count + jnp.arange(
        (reach_count + 1) * row_count, dtype=jnp.int32
    )
    allowed = visible(positions, file_row, key_pos, key_files)
    queries = q_rot.reshape(row_count, kheads, group_size, HEAD_WIDTH)
    out_grads = d_out[0].reshape(row_count, kheads, group_size, HEAD_WIDTH)
    logit_scores = scores_of(queries, key_rows, allowed)
    row_peak = jnp.max(logit_scores, axis=-1, keepdims=True)
    log_total = (
        row_peak + jnp.log(jnp.sum(jnp.exp(logit_scores - row_peak), axis=-1, keepdims=True))
    )[..., 0]
    weights = jnp.exp(logit_scores - log_total[..., None])
    weights_low = weights.astype(jnp.bfloat16)
    attended = jnp.einsum(
        "hgqk,khd->qhgd", weights_low, value_rows, preferred_element_type=jnp.float32
    ).astype(jnp.bfloat16)
    row_delta = jnp.einsum(
        "qhgd,qhgd->hgq", out_grads.astype(jnp.float32), attended.astype(jnp.float32)
    )
    dprobs = jnp.einsum("qhgd,khd->hgqk", out_grads, value_rows, preferred_element_type=jnp.float32)
    dscores = (weights * (dprobs - row_delta[..., None])).astype(jnp.bfloat16)
    grad_queries = scale_factor * jnp.einsum(
        "hgqk,khd->qhgd", dscores, key_rows, preferred_element_type=jnp.float32
    )
    grad_keys = scale_factor * jnp.einsum(
        "hgqk,qhgd->khd", dscores, queries, preferred_element_type=jnp.float32
    )
    grad_values = jnp.einsum(
        "hgqk,qhgd->khd", weights_low, out_grads, preferred_element_type=jnp.float32
    )
    key_own = grad_keys[reach_count * row_count :]
    value_grad = grad_values[reach_count * row_count :]
    for offset in range(1, reach_count + 1):
        low_row = (reach_count - offset) * row_count
        back_keys, back_values = passed_along(
            (grad_keys[low_row : low_row + row_count], grad_values[low_row : low_row + row_count]),
            "ctx",
            -offset,
        )
        key_own = key_own + back_keys
        value_grad = value_grad + back_values
    dq_grad, q_term = restore(
        grad_queries.reshape(row_count, qheads, HEAD_WIDTH), q_unit, q_inv, q_gain, positions
    )
    dk_grad, k_term = restore(key_own, k_unit, k_inv, k_gain, positions)
    gain_terms = jnp.concatenate([q_term, k_term])
    for axis in ("head", "ctx", "fsdp"):
        gain_terms = butterfly_sum(gain_terms, axis)
    q_total, k_total = gain_terms[:HEAD_WIDTH], gain_terms[HEAD_WIDTH:]
    return (
        attended.reshape(1, row_count, -1),
        dq_grad.astype(jnp.bfloat16).reshape(1, row_count, -1),
        dk_grad.astype(jnp.bfloat16).reshape(1, row_count, -1),
        value_grad.astype(jnp.bfloat16).reshape(1, row_count, -1),
        q_total,
        k_total,
    )


def solution(mesh):
    in_specs = (
        P("fsdp", "ctx", "head"),
        P("fsdp", "ctx", "head"),
        P("fsdp", "ctx", "head"),
        P("fsdp", "ctx", "head"),
        P("fsdp", "ctx"),
        P(),
        P(),
    )
    out_specs = (
        P("fsdp", "ctx", "head"),
        P("fsdp", "ctx", "head"),
        P("fsdp", "ctx", "head"),
        P("fsdp", "ctx", "head"),
        P(),
        P(),
    )
    return jax.shard_map(body, mesh=mesh, in_specs=in_specs, out_specs=out_specs, check_vma=False)
```

```python
import jax
import jax.numpy as jnp
from jax import lax
from jax.sharding import PartitionSpec as P

HEAD_WIDTH = 128
WINDOW = 256
QPAS = 168


EPSILON = 1e-06
THETA_BASE = 10000.0
NEGATIVE = -1e30


def passed_along(value, axis, by):
    devices = lax.axis_size(axis)
    pairs = [(i, i + by) for i in range(devices) if 0 <= i + by < devices]
    return lax.ppermute(value, axis, pairs)


def butterfly_sum(value, axis):
    devices = lax.axis_size(axis)
    stride = 1
    while stride < devices:
        pairs = [(i, i ^ stride) for i in range(devices)]
        value = value + lax.ppermute(value, axis, pairs)
        stride *= 2
    return value


def rotate(values, positions):
    half_dim = values.shape[-1] // 2
    frequency = THETA_BASE ** (-(jnp.arange(half_dim, dtype=jnp.float32) * 2.0 / values.shape[-1]))
    angles = positions.astype(jnp.float32)[:, None] * frequency[None, :]
    cosine = jnp.cos(angles)[:, None, :]
    sine_part = jnp.sin(angles)[:, None, :]
    first_half = values[..., :half_dim]
    second = values[..., half_dim:]
    return jnp.concatenate(
        [first_half * cosine - second * sine_part, second * cosine + first_half * sine_part],
        axis=-1,
    )


def unrotate(values, positions):
    half_dim = values.shape[-1] // 2
    frequency = THETA_BASE ** (-(jnp.arange(half_dim, dtype=jnp.float32) * 2.0 / values.shape[-1]))
    angles = positions.astype(jnp.float32)[:, None] * frequency[None, :]
    cosine = jnp.cos(angles)[:, None, :]
    sine_part = jnp.sin(angles)[:, None, :]
    first_half = values[..., :half_dim]
    second = values[..., half_dim:]
    return jnp.concatenate(
        [first_half * cosine + second * sine_part, second * cosine - first_half * sine_part],
        axis=-1,
    )


def normalize(raw_rows, gain_row, positions, head_count):
    values = raw_rows.astype(jnp.float32).reshape(raw_rows.shape[0], head_count, -1)
    inverse = lax.rsqrt(jnp.mean(values * values, axis=-1, keepdims=True) + EPSILON)
    unit_rows = values * inverse
    return (unit_rows, inverse, rotate(unit_rows * gain_row, positions).astype(jnp.bfloat16))


def restore(grad_rot, unit_rows, inverse, gain_row, positions):
    normed = unrotate(grad_rot, positions)
    gain_term = jnp.sum(normed * unit_rows, axis=(0, 1))
    scaled = normed * gain_row
    grad_raw = inverse * (scaled - unit_rows * jnp.mean(scaled * unit_rows, axis=-1, keepdims=True))
    return (grad_raw, gain_term)


def visible(query_pos, query_file, key_pos, key_file):
    earlier = key_pos[None, :] <= query_pos[:, None]
    inside = query_pos[:, None] - key_pos[None, :] < WINDOW
    same_file = key_file[None, :] == query_file[:, None]
    return earlier & inside & same_file & (key_pos[None, :] >= 0)


def scores_of(queries, key_rows, allowed):
    logit_scores = QPAS ** (-0.5) * jnp.einsum(
        "qhgd,khd->hgqk", queries, key_rows, preferred_element_type=jnp.float32
    )
    return jnp.where(allowed[None, None], logit_scores, NEGATIVE)


def body(q_raw, unnormed_keys, value_input, d_out, file_ids, q_gain, k_gain):
    row_count = q_raw.shape[1]
    qheads = q_raw.shape[2] // HEAD_WIDTH
    kheads = unnormed_keys.shape[2] // HEAD_WIDTH
    group_size = qheads // kheads
    ctx_size = lax.axis_size("ctx")
    ctx_place = lax.axis_index("ctx")
    reach_count = min((WINDOW + row_count - 1) // row_count, ctx_size - 1)
    scale_factor = QPAS ** (-0.5)
    positions = ctx_place * row_count + jnp.arange(row_count, dtype=jnp.int32)
    file_row = file_ids[0]
    q_unit, q_inv, q_rot = normalize(q_raw[0], q_gain, positions, qheads)
    k_unit, k_inv, k_rot = normalize(unnormed_keys[0], k_gain, positions, kheads)
    value_own = value_input[0].reshape(row_count, kheads, HEAD_WIDTH)
    file_slab = jnp.broadcast_to(
        file_row.astype(jnp.bfloat16)[None, None, :], (1, 2 * kheads, HEAD_WIDTH)
    )
    packed = jnp.concatenate([jnp.concatenate([k_rot, value_own], axis=1), file_slab], axis=0)
    key_list, value_list, file_list = ([], [], [])
    for offset in range(reach_count, 0, -1):
        far = passed_along(packed, "ctx", offset)
        key_list.append(far[:row_count, :kheads])
        value_list.append(far[:row_count, kheads:])
        file_list.append(far[row_count, 0, :row_count].astype(jnp.int32))
    key_rows = jnp.concatenate(key_list + [k_rot], axis=0)
    value_rows = jnp.concatenate(value_list + [value_own], axis=0)
    key_files = jnp.concatenate(file_list + [file_row], axis=0)
    key_pos = (ctx_place - reach_count) * row_count + jnp.arange(
        (reach_count + 1) * row_count, dtype=jnp.int32
    )
    allowed = visible(positions, file_row, key_pos, key_files)
    queries = q_rot.reshape(row_count, kheads, group_size, HEAD_WIDTH)
    out_grads = d_out[0].reshape(row_count, kheads, group_size, HEAD_WIDTH)
    logit_scores = scores_of(queries, key_rows, allowed)
    row_peak = jnp.max(logit_scores, axis=-1, keepdims=True)
    log_total = (
        row_peak + jnp.log(jnp.sum(jnp.exp(logit_scores - row_peak), axis=-1, keepdims=True))
    )[..., 0]
    weights = jnp.exp(logit_scores - log_total[..., None])
    weights_low = weights.astype(jnp.bfloat16)
    attended = jnp.einsum(
        "hgqk,khd->qhgd", weights_low, value_rows, preferred_element_type=jnp.float32
    ).astype(jnp.bfloat16)
    row_delta = jnp.einsum(
        "qhgd,qhgd->hgq", out_grads.astype(jnp.float32), attended.astype(jnp.float32)
    )
    dprobs = jnp.einsum("qhgd,khd->hgqk", out_grads, value_rows, preferred_element_type=jnp.float32)
    dscores = (weights * (dprobs - row_delta[..., None])).astype(jnp.bfloat16)
    grad_queries = scale_factor * jnp.einsum(
        "hgqk,khd->qhgd", dscores, key_rows, preferred_element_type=jnp.float32
    )
    grad_keys = scale_factor * jnp.einsum(
        "hgqk,qhgd->khd", dscores, queries, preferred_element_type=jnp.float32
    )
    grad_values = jnp.einsum(
        "hgqk,qhgd->khd", weights_low, out_grads, preferred_element_type=jnp.float32
    )
    key_own = grad_keys[reach_count * row_count :]
    value_grad = grad_values[reach_count * row_count :]
    for offset in range(1, reach_count + 1):
        low_row = (reach_count - offset) * row_count
        back = passed_along(
            jnp.concatenate(
                [grad_keys[low_row : low_row + row_count], grad_values[low_row : low_row + row_count]],
                axis=1,
            ),
            "ctx",
            -offset,
        )
        back_keys, back_values = back[:, :kheads], back[:, kheads:]
        key_own = key_own + back_keys
        value_grad = value_grad + back_values
    dq_grad, q_term = restore(
        grad_queries.reshape(row_count, qheads, HEAD_WIDTH), q_unit, q_inv, q_gain, positions
    )
    dk_grad, k_term = restore(key_own, k_unit, k_inv, k_gain, positions)
    gain_terms = jnp.concatenate([q_term, k_term])
    for axis in ("head", "ctx", "fsdp"):
        gain_terms = butterfly_sum(gain_terms, axis)
    q_total, k_total = gain_terms[:HEAD_WIDTH], gain_terms[HEAD_WIDTH:]
    return (
        attended.reshape(1, row_count, -1),
        dq_grad.astype(jnp.bfloat16).reshape(1, row_count, -1),
        dk_grad.astype(jnp.bfloat16).reshape(1, row_count, -1),
        value_grad.astype(jnp.bfloat16).reshape(1, row_count, -1),
        q_total,
        k_total,
    )


def solution(mesh):
    in_specs = (
        P("fsdp", "ctx", "head"),
        P("fsdp", "ctx", "head"),
        P("fsdp", "ctx", "head"),
        P("fsdp", "ctx", "head"),
        P("fsdp", "ctx"),
        P(),
        P(),
    )
    out_specs = (
        P("fsdp", "ctx", "head"),
        P("fsdp", "ctx", "head"),
        P("fsdp", "ctx", "head"),
        P("fsdp", "ctx", "head"),
        P(),
        P(),
    )
    return jax.shard_map(body, mesh=mesh, in_specs=in_specs, out_specs=out_specs, check_vma=False)
```

```python
import jax
import jax.numpy as jnp
from jax import lax
from jax.sharding import PartitionSpec as P

HEAD_WIDTH = 128
WINDOW = 256
QPAS = 168


EPSILON = 1e-06
THETA_BASE = 10000.0
NEGATIVE = -1e30


def passed_along(value, axis, by):
    devices = lax.axis_size(axis)
    pairs = [(i, i + by) for i in range(devices) if 0 <= i + by < devices]
    return lax.ppermute(value, axis, pairs)


def butterfly_sum(value, axis):
    devices = lax.axis_size(axis)
    stride = 1
    while stride < devices:
        pairs = [(i, i ^ stride) for i in range(devices)]
        value = value + lax.ppermute(value, axis, pairs)
        stride *= 2
    return value


def rotate(values, positions):
    half_dim = values.shape[-1] // 2
    frequency = THETA_BASE ** (-(jnp.arange(half_dim, dtype=jnp.float32) * 2.0 / values.shape[-1]))
    angles = positions.astype(jnp.float32)[:, None] * frequency[None, :]
    cosine = jnp.cos(angles)[:, None, :]
    sine_part = jnp.sin(angles)[:, None, :]
    first_half = values[..., :half_dim]
    second = values[..., half_dim:]
    return jnp.concatenate(
        [first_half * cosine - second * sine_part, second * cosine + first_half * sine_part],
        axis=-1,
    )


def unrotate(values, positions):
    half_dim = values.shape[-1] // 2
    frequency = THETA_BASE ** (-(jnp.arange(half_dim, dtype=jnp.float32) * 2.0 / values.shape[-1]))
    angles = positions.astype(jnp.float32)[:, None] * frequency[None, :]
    cosine = jnp.cos(angles)[:, None, :]
    sine_part = jnp.sin(angles)[:, None, :]
    first_half = values[..., :half_dim]
    second = values[..., half_dim:]
    return jnp.concatenate(
        [first_half * cosine + second * sine_part, second * cosine - first_half * sine_part],
        axis=-1,
    )


def normalize(raw_rows, gain_row, positions, head_count):
    values = raw_rows.astype(jnp.float32).reshape(raw_rows.shape[0], head_count, -1)
    inverse = lax.rsqrt(jnp.mean(values * values, axis=-1, keepdims=True) + EPSILON)
    unit_rows = values * inverse
    return (unit_rows, inverse, rotate(unit_rows * gain_row, positions).astype(jnp.bfloat16))


def restore(grad_rot, unit_rows, inverse, gain_row, positions):
    normed = unrotate(grad_rot, positions)
    gain_term = jnp.sum(normed * unit_rows, axis=(0, 1))
    scaled = normed * gain_row
    grad_raw = inverse * (scaled - unit_rows * jnp.mean(scaled * unit_rows, axis=-1, keepdims=True))
    return (grad_raw, gain_term)


def visible(query_pos, query_file, key_pos, key_file):
    earlier = key_pos[None, :] <= query_pos[:, None]
    inside = query_pos[:, None] - key_pos[None, :] < WINDOW
    same_file = key_file[None, :] == query_file[:, None]
    return earlier & inside & same_file & (key_pos[None, :] >= 0)


def scores_of(queries, key_rows, allowed):
    logit_scores = QPAS ** (-0.5) * jnp.einsum(
        "qhgd,khd->hgqk", queries, key_rows, preferred_element_type=jnp.float32
    )
    return jnp.where(allowed[None, None], logit_scores, NEGATIVE)


def body(q_raw, unnormed_keys, value_input, d_out, file_ids, q_gain, k_gain):
    row_count = q_raw.shape[1]
    qheads = q_raw.shape[2] // HEAD_WIDTH
    kheads = unnormed_keys.shape[2] // HEAD_WIDTH
    group_size = qheads // kheads
    ctx_size = lax.axis_size("ctx")
    ctx_place = lax.axis_index("ctx")
    reach_count = min((WINDOW + row_count - 1) // row_count, ctx_size - 1)
    scale_factor = QPAS ** (-0.5)
    positions = ctx_place * row_count + jnp.arange(row_count, dtype=jnp.int32)
    file_row = file_ids[0]
    q_unit, q_inv, q_rot = normalize(q_raw[0], q_gain, positions, qheads)
    k_unit, k_inv, k_rot = normalize(unnormed_keys[0], k_gain, positions, kheads)
    value_own = value_input[0].reshape(row_count, kheads, HEAD_WIDTH)
    file_slab = jnp.broadcast_to(
        file_row.astype(jnp.bfloat16)[None, None, :], (1, 2 * kheads, HEAD_WIDTH)
    )
    packed = jnp.concatenate([jnp.concatenate([k_rot, value_own], axis=1), file_slab], axis=0)
    key_list, value_list, file_list = ([], [], [])
    for offset in range(reach_count, 0, -1):
        far = passed_along(packed, "ctx", offset)
        key_list.append(far[:row_count, :kheads])
        value_list.append(far[:row_count, kheads:])
        file_list.append(far[row_count, 0, :row_count].astype(jnp.int32))
    key_rows = jnp.concatenate(key_list + [k_rot], axis=0)
    value_rows = jnp.concatenate(value_list + [value_own], axis=0)
    key_files = jnp.concatenate(file_list + [file_row], axis=0)
    key_pos = (ctx_place - reach_count) * row_count + jnp.arange(
        (reach_count + 1) * row_count, dtype=jnp.int32
    )
    allowed = visible(positions, file_row, key_pos, key_files)
    queries = q_rot.reshape(row_count, kheads, group_size, HEAD_WIDTH)
    out_grads = d_out[0].reshape(row_count, kheads, group_size, HEAD_WIDTH)
    logit_scores = scores_of(queries, key_rows, allowed)
    row_peak = jnp.max(logit_scores, axis=-1, keepdims=True)
    log_total = (
        row_peak + jnp.log(jnp.sum(jnp.exp(logit_scores - row_peak), axis=-1, keepdims=True))
    )[..., 0]
    weights = jnp.exp(logit_scores - log_total[..., None])
    weights_low = weights.astype(jnp.bfloat16)
    attended = jnp.einsum(
        "hgqk,khd->qhgd", weights_low, value_rows, preferred_element_type=jnp.float32
    ).astype(jnp.bfloat16)
    row_delta = jnp.einsum(
        "qhgd,qhgd->hgq", out_grads.astype(jnp.float32), attended.astype(jnp.float32)
    )
    dprobs = jnp.einsum("qhgd,khd->hgqk", out_grads, value_rows, preferred_element_type=jnp.float32)
    dscores = (weights * (dprobs - row_delta[..., None])).astype(jnp.bfloat16)
    grad_queries = scale_factor * jnp.einsum(
        "hgqk,khd->qhgd", dscores, key_rows, preferred_element_type=jnp.float32
    )
    grad_keys = scale_factor * jnp.einsum(
        "hgqk,qhgd->khd", dscores, queries, preferred_element_type=jnp.float32
    )
    grad_values = jnp.einsum(
        "hgqk,qhgd->khd", weights_low, out_grads, preferred_element_type=jnp.float32
    )
    key_own = grad_keys[reach_count * row_count :]
    value_grad = grad_values[reach_count * row_count :]
    for offset in range(1, reach_count + 1):
        low_row = (reach_count - offset) * row_count
        back_keys = passed_along(
            grad_keys[low_row : low_row + row_count].astype(jnp.bfloat16), "ctx", -offset
        ).astype(jnp.float32)
        back_values = passed_along(grad_values[low_row : low_row + row_count], "ctx", -offset)
        key_own = key_own + back_keys
        value_grad = value_grad + back_values
    dq_grad, q_term = restore(
        grad_queries.reshape(row_count, qheads, HEAD_WIDTH), q_unit, q_inv, q_gain, positions
    )
    dk_grad, k_term = restore(key_own, k_unit, k_inv, k_gain, positions)
    gain_terms = jnp.concatenate([q_term, k_term])
    for axis in ("head", "ctx", "fsdp"):
        gain_terms = butterfly_sum(gain_terms, axis)
    q_total, k_total = gain_terms[:HEAD_WIDTH], gain_terms[HEAD_WIDTH:]
    return (
        attended.reshape(1, row_count, -1),
        dq_grad.astype(jnp.bfloat16).reshape(1, row_count, -1),
        dk_grad.astype(jnp.bfloat16).reshape(1, row_count, -1),
        value_grad.astype(jnp.bfloat16).reshape(1, row_count, -1),
        q_total,
        k_total,
    )


def solution(mesh):
    in_specs = (
        P("fsdp", "ctx", "head"),
        P("fsdp", "ctx", "head"),
        P("fsdp", "ctx", "head"),
        P("fsdp", "ctx", "head"),
        P("fsdp", "ctx"),
        P(),
        P(),
    )
    out_specs = (
        P("fsdp", "ctx", "head"),
        P("fsdp", "ctx", "head"),
        P("fsdp", "ctx", "head"),
        P("fsdp", "ctx", "head"),
        P(),
        P(),
    )
    return jax.shard_map(body, mesh=mesh, in_specs=in_specs, out_specs=out_specs, check_vma=False)
```

```python
import jax
import jax.numpy as jnp
from jax import lax
from jax.sharding import PartitionSpec as P

HEAD_WIDTH = 128
WINDOW = 256
QPAS = 168


EPSILON = 1e-06
THETA_BASE = 10000.0
NEGATIVE = -1e30


def passed_along(value, axis, by):
    devices = lax.axis_size(axis)
    pairs = [(i, i + by) for i in range(devices) if 0 <= i + by < devices]
    return lax.ppermute(value, axis, pairs)


def butterfly_sum(value, axis):
    devices = lax.axis_size(axis)
    stride = 1
    while stride < devices:
        pairs = [(i, i ^ stride) for i in range(devices)]
        value = value + lax.ppermute(value, axis, pairs)
        stride *= 2
    return value


def rotate(values, positions):
    half_dim = values.shape[-1] // 2
    frequency = THETA_BASE ** (-(jnp.arange(half_dim, dtype=jnp.float32) * 2.0 / values.shape[-1]))
    angles = positions.astype(jnp.float32)[:, None] * frequency[None, :]
    cosine = jnp.cos(angles)[:, None, :]
    sine_part = jnp.sin(angles)[:, None, :]
    first_half = values[..., :half_dim]
    second = values[..., half_dim:]
    return jnp.concatenate(
        [first_half * cosine - second * sine_part, second * cosine + first_half * sine_part],
        axis=-1,
    )


def unrotate(values, positions):
    half_dim = values.shape[-1] // 2
    frequency = THETA_BASE ** (-(jnp.arange(half_dim, dtype=jnp.float32) * 2.0 / values.shape[-1]))
    angles = positions.astype(jnp.float32)[:, None] * frequency[None, :]
    cosine = jnp.cos(angles)[:, None, :]
    sine_part = jnp.sin(angles)[:, None, :]
    first_half = values[..., :half_dim]
    second = values[..., half_dim:]
    return jnp.concatenate(
        [first_half * cosine + second * sine_part, second * cosine - first_half * sine_part],
        axis=-1,
    )


def normalize(raw_rows, gain_row, positions, head_count):
    values = raw_rows.astype(jnp.float32).reshape(raw_rows.shape[0], head_count, -1)
    inverse = lax.rsqrt(jnp.mean(values * values, axis=-1, keepdims=True) + EPSILON)
    unit_rows = values * inverse
    return (unit_rows, inverse, rotate(unit_rows * gain_row, positions).astype(jnp.bfloat16))


def restore(grad_rot, unit_rows, inverse, gain_row, positions):
    normed = unrotate(grad_rot, positions)
    gain_term = jnp.sum(normed * unit_rows, axis=(0, 1))
    scaled = normed * gain_row
    grad_raw = inverse * (scaled - unit_rows * jnp.mean(scaled * unit_rows, axis=-1, keepdims=True))
    return (grad_raw, gain_term)


def visible(query_pos, query_file, key_pos, key_file):
    earlier = key_pos[None, :] <= query_pos[:, None]
    inside = query_pos[:, None] - key_pos[None, :] < WINDOW
    same_file = key_file[None, :] == query_file[:, None]
    return earlier & inside & same_file & (key_pos[None, :] >= 0)


def scores_of(queries, key_rows, allowed):
    logit_scores = QPAS ** (-0.5) * jnp.einsum(
        "qhgd,khd->hgqk", queries, key_rows, preferred_element_type=jnp.float32
    )
    return jnp.where(allowed[None, None], logit_scores, NEGATIVE)


def body(q_raw, unnormed_keys, value_input, d_out, file_ids, q_gain, k_gain):
    row_count = q_raw.shape[1]
    qheads = q_raw.shape[2] // HEAD_WIDTH
    kheads = unnormed_keys.shape[2] // HEAD_WIDTH
    group_size = qheads // kheads
    ctx_size = lax.axis_size("ctx")
    ctx_place = lax.axis_index("ctx")
    reach_count = min((WINDOW + row_count - 1) // row_count, ctx_size - 1)
    scale_factor = QPAS ** (-0.5)
    positions = ctx_place * row_count + jnp.arange(row_count, dtype=jnp.int32)
    file_row = file_ids[0]
    q_unit, q_inv, q_rot = normalize(q_raw[0], q_gain, positions, qheads)
    k_unit, k_inv, k_rot = normalize(unnormed_keys[0], k_gain, positions, kheads)
    value_own = value_input[0].reshape(row_count, kheads, HEAD_WIDTH)
    file_slab = jnp.broadcast_to(
        file_row.astype(jnp.bfloat16)[None, None, :], (1, 2 * kheads, HEAD_WIDTH)
    )
    packed = jnp.concatenate([jnp.concatenate([k_rot, value_own], axis=1), file_slab], axis=0)
    key_list, value_list, file_list, unit_list = ([], [], [], [])
    for offset in range(reach_count, 0, -1):
        unit_list.append(passed_along(k_unit, "ctx", offset))
        far = passed_along(packed, "ctx", offset)
        key_list.append(far[:row_count, :kheads])
        value_list.append(far[:row_count, kheads:])
        file_list.append(far[row_count, 0, :row_count].astype(jnp.int32))
    key_rows = jnp.concatenate(key_list + [k_rot], axis=0)
    value_rows = jnp.concatenate(value_list + [value_own], axis=0)
    key_files = jnp.concatenate(file_list + [file_row], axis=0)
    key_pos = (ctx_place - reach_count) * row_count + jnp.arange(
        (reach_count + 1) * row_count, dtype=jnp.int32
    )
    allowed = visible(positions, file_row, key_pos, key_files)
    queries = q_rot.reshape(row_count, kheads, group_size, HEAD_WIDTH)
    out_grads = d_out[0].reshape(row_count, kheads, group_size, HEAD_WIDTH)
    logit_scores = scores_of(queries, key_rows, allowed)
    row_peak = jnp.max(logit_scores, axis=-1, keepdims=True)
    log_total = (
        row_peak + jnp.log(jnp.sum(jnp.exp(logit_scores - row_peak), axis=-1, keepdims=True))
    )[..., 0]
    weights = jnp.exp(logit_scores - log_total[..., None])
    weights_low = weights.astype(jnp.bfloat16)
    attended = jnp.einsum(
        "hgqk,khd->qhgd", weights_low, value_rows, preferred_element_type=jnp.float32
    ).astype(jnp.bfloat16)
    row_delta = jnp.einsum(
        "qhgd,qhgd->hgq", out_grads.astype(jnp.float32), attended.astype(jnp.float32)
    )
    dprobs = jnp.einsum("qhgd,khd->hgqk", out_grads, value_rows, preferred_element_type=jnp.float32)
    dscores = (weights * (dprobs - row_delta[..., None])).astype(jnp.bfloat16)
    grad_queries = scale_factor * jnp.einsum(
        "hgqk,khd->qhgd", dscores, key_rows, preferred_element_type=jnp.float32
    )
    grad_keys = scale_factor * jnp.einsum(
        "hgqk,qhgd->khd", dscores, queries, preferred_element_type=jnp.float32
    )
    grad_values = jnp.einsum(
        "hgqk,qhgd->khd", weights_low, out_grads, preferred_element_type=jnp.float32
    )
    key_units = jnp.concatenate(unit_list + [k_unit], axis=0)
    k_term = jnp.sum(unrotate(grad_keys, key_pos) * key_units, axis=(0, 1))
    key_own = grad_keys[reach_count * row_count :]
    value_grad = grad_values[reach_count * row_count :]
    for offset in range(1, reach_count + 1):
        low_row = (reach_count - offset) * row_count
        back_keys = passed_along(
            grad_keys[low_row : low_row + row_count].astype(jnp.bfloat16), "ctx", -offset
        ).astype(jnp.float32)
        back_values = passed_along(grad_values[low_row : low_row + row_count], "ctx", -offset)
        key_own = key_own + back_keys
        value_grad = value_grad + back_values
    dq_grad, q_term = restore(
        grad_queries.reshape(row_count, qheads, HEAD_WIDTH), q_unit, q_inv, q_gain, positions
    )
    dk_grad, _ = restore(key_own, k_unit, k_inv, k_gain, positions)
    gain_terms = jnp.concatenate([q_term, k_term])
    for axis in ("head", "ctx", "fsdp"):
        gain_terms = butterfly_sum(gain_terms, axis)
    q_total, k_total = gain_terms[:HEAD_WIDTH], gain_terms[HEAD_WIDTH:]
    return (
        attended.reshape(1, row_count, -1),
        dq_grad.astype(jnp.bfloat16).reshape(1, row_count, -1),
        dk_grad.astype(jnp.bfloat16).reshape(1, row_count, -1),
        value_grad.astype(jnp.bfloat16).reshape(1, row_count, -1),
        q_total,
        k_total,
    )


def solution(mesh):
    in_specs = (
        P("fsdp", "ctx", "head"),
        P("fsdp", "ctx", "head"),
        P("fsdp", "ctx", "head"),
        P("fsdp", "ctx", "head"),
        P("fsdp", "ctx"),
        P(),
        P(),
    )
    out_specs = (
        P("fsdp", "ctx", "head"),
        P("fsdp", "ctx", "head"),
        P("fsdp", "ctx", "head"),
        P("fsdp", "ctx", "head"),
        P(),
        P(),
    )
    return jax.shard_map(body, mesh=mesh, in_specs=in_specs, out_specs=out_specs, check_vma=False)
```

```python
import jax
import jax.numpy as jnp
from jax import lax
from jax.sharding import PartitionSpec as P

HEAD_WIDTH = 128
WINDOW = 256
QPAS = 168


EPSILON = 1e-06
THETA_BASE = 10000.0
NEGATIVE = -1e30


def passed_along(value, axis, by):
    devices = lax.axis_size(axis)
    pairs = [(i, i + by) for i in range(devices) if 0 <= i + by < devices]
    return lax.ppermute(value, axis, pairs)


def butterfly_sum(value, axis):
    devices = lax.axis_size(axis)
    stride = 1
    while stride < devices:
        pairs = [(i, i ^ stride) for i in range(devices)]
        value = value + lax.ppermute(value, axis, pairs)
        stride *= 2
    return value


def rotate(values, positions):
    half_dim = values.shape[-1] // 2
    frequency = THETA_BASE ** (-(jnp.arange(half_dim, dtype=jnp.float32) * 2.0 / values.shape[-1]))
    angles = positions.astype(jnp.float32)[:, None] * frequency[None, :]
    cosine = jnp.cos(angles)[:, None, :]
    sine_part = jnp.sin(angles)[:, None, :]
    first_half = values[..., :half_dim]
    second = values[..., half_dim:]
    return jnp.concatenate(
        [first_half * cosine - second * sine_part, second * cosine + first_half * sine_part],
        axis=-1,
    )


def unrotate(values, positions):
    half_dim = values.shape[-1] // 2
    frequency = THETA_BASE ** (-(jnp.arange(half_dim, dtype=jnp.float32) * 2.0 / values.shape[-1]))
    angles = positions.astype(jnp.float32)[:, None] * frequency[None, :]
    cosine = jnp.cos(angles)[:, None, :]
    sine_part = jnp.sin(angles)[:, None, :]
    first_half = values[..., :half_dim]
    second = values[..., half_dim:]
    return jnp.concatenate(
        [first_half * cosine + second * sine_part, second * cosine - first_half * sine_part],
        axis=-1,
    )


def normalize(raw_rows, gain_row, positions, head_count):
    values = raw_rows.astype(jnp.float32).reshape(raw_rows.shape[0], head_count, -1)
    inverse = lax.rsqrt(jnp.mean(values * values, axis=-1, keepdims=True) + EPSILON)
    unit_rows = values * inverse
    return (unit_rows, inverse, rotate(unit_rows * gain_row, positions).astype(jnp.bfloat16))


def restore(grad_rot, unit_rows, inverse, gain_row, positions):
    normed = unrotate(grad_rot, positions)
    gain_term = jnp.sum(normed * unit_rows, axis=(0, 1))
    scaled = normed * gain_row
    grad_raw = inverse * (scaled - unit_rows * jnp.mean(scaled * unit_rows, axis=-1, keepdims=True))
    return (grad_raw, gain_term)


def visible(query_pos, query_file, key_pos, key_file):
    earlier = key_pos[None, :] <= query_pos[:, None]
    inside = query_pos[:, None] - key_pos[None, :] < WINDOW
    same_file = key_file[None, :] == query_file[:, None]
    return earlier & inside & same_file & (key_pos[None, :] >= 0)


def scores_of(queries, key_rows, allowed):
    logit_scores = QPAS ** (-0.5) * jnp.einsum(
        "qhgd,khd->hgqk", queries, key_rows, preferred_element_type=jnp.float32
    )
    return jnp.where(allowed[None, None], logit_scores, NEGATIVE)


def body(q_raw, unnormed_keys, value_input, d_out, file_ids, q_gain, k_gain):
    row_count = q_raw.shape[1]
    qheads = q_raw.shape[2] // HEAD_WIDTH
    kheads = unnormed_keys.shape[2] // HEAD_WIDTH
    group_size = qheads // kheads
    ctx_size = lax.axis_size("ctx")
    ctx_place = lax.axis_index("ctx")
    reach_count = min((WINDOW + row_count - 1) // row_count, ctx_size - 1)
    scale_factor = QPAS ** (-0.5)
    positions = ctx_place * row_count + jnp.arange(row_count, dtype=jnp.int32)
    file_row = file_ids[0]
    q_unit, q_inv, q_rot = normalize(q_raw[0], q_gain, positions, qheads)
    k_unit, k_inv, k_rot = normalize(unnormed_keys[0], k_gain, positions, kheads)
    value_own = value_input[0].reshape(row_count, kheads, HEAD_WIDTH)
    file_slab = jnp.broadcast_to(
        file_row.astype(jnp.bfloat16)[None, None, :], (1, 2 * kheads, HEAD_WIDTH)
    )
    packed = jnp.concatenate([jnp.concatenate([k_rot, value_own], axis=1), file_slab], axis=0)
    key_list, value_list, file_list = ([], [], [])
    for offset in range(reach_count, 0, -1):
        far = passed_along(packed, "ctx", offset)
        key_list.append(far[:row_count, :kheads])
        value_list.append(far[:row_count, kheads:])
        file_list.append(far[row_count, 0, :row_count].astype(jnp.int32))
    key_rows = jnp.concatenate(key_list + [k_rot], axis=0)
    value_rows = jnp.concatenate(value_list + [value_own], axis=0)
    key_files = jnp.concatenate(file_list + [file_row], axis=0)
    key_pos = (ctx_place - reach_count) * row_count + jnp.arange(
        (reach_count + 1) * row_count, dtype=jnp.int32
    )
    allowed = visible(positions, file_row, key_pos, key_files)
    queries = q_rot.reshape(row_count, kheads, group_size, HEAD_WIDTH)
    out_grads = d_out[0].reshape(row_count, kheads, group_size, HEAD_WIDTH)
    logit_scores = scores_of(queries, key_rows, allowed)
    row_peak = jnp.max(logit_scores, axis=-1, keepdims=True)
    log_total = (
        row_peak + jnp.log(jnp.sum(jnp.exp(logit_scores - row_peak), axis=-1, keepdims=True))
    )[..., 0]
    weights = jnp.exp(logit_scores - log_total[..., None])
    weights_low = weights.astype(jnp.bfloat16)
    attended = jnp.einsum(
        "hgqk,khd->qhgd", weights_low, value_rows, preferred_element_type=jnp.float32
    ).astype(jnp.bfloat16)
    row_delta = jnp.einsum(
        "qhgd,qhgd->hgq", out_grads.astype(jnp.float32), attended.astype(jnp.float32)
    )
    dprobs = jnp.einsum("qhgd,khd->hgqk", out_grads, value_rows, preferred_element_type=jnp.float32)
    dscores = (weights * (dprobs - row_delta[..., None])).astype(jnp.bfloat16)
    grad_queries = scale_factor * jnp.einsum(
        "hgqk,khd->qhgd", dscores, key_rows, preferred_element_type=jnp.float32
    )
    grad_keys = scale_factor * jnp.einsum(
        "hgqk,qhgd->khd", dscores, queries, preferred_element_type=jnp.float32
    )
    grad_values = jnp.einsum(
        "hgqk,qhgd->khd", weights_low, out_grads, preferred_element_type=jnp.float32
    )
    key_own = grad_keys[reach_count * row_count :]
    value_grad = grad_values[reach_count * row_count :]
    for offset in range(1, reach_count + 1):
        low_row = (reach_count - offset) * row_count
        back_keys = passed_along(
            grad_keys[low_row : low_row + row_count].astype(jnp.bfloat16), "ctx", -offset
        ).astype(jnp.float32)
        back_values = passed_along(
            grad_values[low_row : low_row + row_count].astype(jnp.bfloat16), "ctx", -offset
        ).astype(jnp.float32)
        key_own = key_own + back_keys
        value_grad = value_grad + back_values
    dq_grad, q_term = restore(
        grad_queries.reshape(row_count, qheads, HEAD_WIDTH), q_unit, q_inv, q_gain, positions
    )
    dk_grad, k_term = restore(key_own, k_unit, k_inv, k_gain, positions)
    gain_terms = jnp.concatenate([q_term, k_term])
    for axis in ("head", "ctx", "fsdp"):
        gain_terms = butterfly_sum(gain_terms, axis)
    q_total, k_total = gain_terms[:HEAD_WIDTH], gain_terms[HEAD_WIDTH:]
    return (
        attended.reshape(1, row_count, -1),
        dq_grad.astype(jnp.bfloat16).reshape(1, row_count, -1),
        dk_grad.astype(jnp.bfloat16).reshape(1, row_count, -1),
        value_grad.astype(jnp.bfloat16).reshape(1, row_count, -1),
        q_total,
        k_total,
    )


def solution(mesh):
    in_specs = (
        P("fsdp", "ctx", "head"),
        P("fsdp", "ctx", "head"),
        P("fsdp", "ctx", "head"),
        P("fsdp", "ctx", "head"),
        P("fsdp", "ctx"),
        P(),
        P(),
    )
    out_specs = (
        P("fsdp", "ctx", "head"),
        P("fsdp", "ctx", "head"),
        P("fsdp", "ctx", "head"),
        P("fsdp", "ctx", "head"),
        P(),
        P(),
    )
    return jax.shard_map(body, mesh=mesh, in_specs=in_specs, out_specs=out_specs, check_vma=False)
```
